128 devices in a mesh: row: 8 (over x, y_hi), col: 16 (over y_lo, z, core).
Axes of the slice: x: 4, y: 4 (y_hi: 2, y_lo: 2; y = y_hi * 2 + y_lo), z: 4, core: 2. Of those that a mesh axis runs over, the one named last changes fastest.
Arguments:
- flat_gradient: bfloat16 [8, 16, 524288], P('row', 'col'), may hold values from -6 to 6
- range_rows: int32 [8, 16], replicated, may hold values from 1 to 64, 512 in all within a row
- left_stat: float32 [4096, 4096], P('row', 'col'), may hold values from -6 to 6
- right_stat: float32 [8192, 8192], P('col', 'row'), may hold values from -6 to 6
- left_root: bfloat16 [4096, 4096], P('row'), as said below
- right_root: bfloat16 [8192, 8192], P('col'), as said below
Outputs:
- left_new: float32 [4096, 4096], P('row', 'col')
- right_new: float32 [8192, 8192], P('col', 'row')
- update: bfloat16 [4096, 8192], P('row', 'col')
The draws below stay inside these ranges and needn't reach their ends.
Inputs may be any that keep to these rules, and one draw needn't show every extreme that they name: In each row r the entries sum to 512; the largest entry of every row is exactly 64. Slots of flat_gradient beyond a device's range_rows rows are padding. left_root equals its transpose. right_root equals its transpose.
All inputs are finite; a program needn't handle non-finite values.
Results may differ from the reference program's by a relative error of at most 0.014.
Values may be sent and summed in bfloat16 or wider, within the bound.
No kernel may reach another device: no remote copies, remote signals or barrier semaphores. Data moves between devices by JAX's collectives and lax.ppermute only.
A program may use at most 192 MiB of HBM per device.

```python
import math
import jax
import jax.numpy as jnp
import numpy as np
from jax import lax

HQ = 4096
DIN = 8192
ROW_TILE = 512
CAPROWS = 64
N_ROW = 8
N_COL = 16


def symmetric_draw(key, order):
    base = jnp.clip(jax.random.normal(key, (order, order), jnp.float32), -4.0, 4.0)
    return ((base + base.T) * (1.0 / math.sqrt(2.0 * order))).astype(jnp.bfloat16)


def draw_left_root(key, part):
    return symmetric_draw(jax.random.fold_in(key, 11), HQ)


def draw_right_root(key, part):
    return symmetric_draw(jax.random.fold_in(key, 23), DIN)


def levels(key, dims, shards, low, largest):
    def one(position, parts):
        steps = jax.random.uniform(jax.random.fold_in(jax.random.fold_in(key, 6), position), (parts,), jnp.float32, low / len(shards), largest / len(shards))
        return jnp.repeat(jnp.exp(steps), dims[position] // parts).reshape((-1,) + (1,) * (len(dims) - position - 1))

    loudness = one(*shards[0])
    for cut in shards[1:]:
        loudness = loudness * one(*cut)
    return loudness


def length_profile(count, total, most, slope):
    weights = [(1 << 20) // math.isqrt(rank ** slope) + 1 for rank in range(2, count + 1)]
    spare, holding = total - most - (count - 1), [1] * (count - 1)
    while spare > 0:
        free = [i for i in range(count - 1) if holding[i] < most]
        whole, left = sum([weights[i] for i in free]), spare
        for i in free:
            addition = min(most - holding[i], max(1, left * weights[i] // whole), spare)
            holding[i] = holding[i] + addition
            spare = spare - addition
    return np.array([most] + holding)


def ragged(rng, number_of, total, reach, slope):
    if number_of == 2:
        one = jax.random.randint(rng, (), max(1, total - reach), min(reach, total - 1) + 1)
        return jnp.stack([one, total - one])
    lengths = jnp.asarray(length_profile(number_of, total, reach, slope), jnp.int32)
    twos = (number_of - 1) // 2
    source_of, taker = lengths[1:1 + 2 * twos:2], lengths[2:2 + 2 * twos:2]
    room = jnp.minimum(source_of - 1, reach - taker)
    moved = jax.random.randint(jax.random.fold_in(rng, 1), (twos,), 0, 1 << 20) % (room + 1)
    lengths = lengths.at[1:1 + 2 * twos:2].set(source_of - moved).at[2:2 + 2 * twos:2].set(taker + moved)
    return lengths[jax.random.permutation(jax.random.fold_in(rng, 2), number_of)]


def normal_values(stream_key, shape, width, reach, shards=(), kind=jnp.bfloat16):
    entries = jax.random.normal(stream_key, shape, jnp.float32) * width
    if len(shards) > 0:
        entries = levels(stream_key, shape, shards, -0.22, 0.18) * entries
    return jnp.clip(entries, min=-reach, max=reach).astype(kind)


def setup_inputs(seed: int = 0) -> dict:
    key_of = jax.random.split(jax.random.key(seed), 7)
    flat_gradient = normal_values(key_of[0], (N_ROW, N_COL, CAPROWS * DIN), 1.0, 6.0, ((0, 8), (1, 16)))
    range_rows = jax.vmap(lambda own: ragged(own, N_COL, ROW_TILE, CAPROWS, 2))(jax.random.split(key_of[1], N_ROW)).reshape((N_ROW, N_COL)).astype(jnp.int32)
    left_stat = normal_values(key_of[2], (HQ, HQ), 1.0, 6.0, ((0, 8), (1, 16)), jnp.float32)
    right_stat = normal_values(key_of[3], (DIN, DIN), 1.0, 6.0, ((0, 16), (1, 8)), jnp.float32)
    left_root = draw_left_root(jax.random.fold_in(key_of[6], 71), 0)
    right_root = draw_right_root(jax.random.fold_in(key_of[6], 71), 0)
    return dict(flat_gradient=flat_gradient, range_rows=range_rows, left_stat=left_stat, right_stat=right_stat, left_root=left_root, right_root=right_root)


stat_decay = 0.9

def slot_index(row_counts, tile_rows, capacity):
    offsets = (jnp.cumsum(row_counts) - row_counts).astype(jnp.int32)
    target = jnp.arange(tile_rows, dtype=jnp.int32)
    covered = target[:, None] >= offsets[None, :]
    source = (lax.optimization_barrier(jnp.sum(covered.astype(jnp.int32), axis=1)) - 1).astype(jnp.int32)
    begins = lax.optimization_barrier(jnp.max(jnp.where(covered, offsets[None, :], 0), axis=1)).astype(jnp.int32)
    return (source * capacity + target - begins).astype(jnp.int32)

def pick_rows(block, chosen):
    return jnp.take(block, chosen, axis=0)

def group_index(row_counts):
    return slot_index(row_counts, ROW_TILE, CAPROWS)

def reference(flat_gradient, range_rows, left_stat, right_stat, left_root, right_root):
    stacked = flat_gradient.reshape(N_ROW, N_COL * CAPROWS, DIN)
    chosen = jax.vmap(group_index)(range_rows.astype(jnp.int32))
    grad = jax.vmap(pick_rows)(stacked, chosen).reshape(HQ, DIN)
    left_gram = jnp.dot(grad, grad.T, preferred_element_type=jnp.float32)
    left_new = stat_decay * left_stat + left_gram * (1.0 / math.sqrt(DIN))
    right_gram = lax.dot_general(grad, grad, (((0,), (0,)), ((), ())), preferred_element_type=jnp.float32)
    right_new = stat_decay * right_stat + right_gram * (1.0 / math.sqrt(HQ))
    mixed = jnp.dot(left_root, grad, preferred_element_type=jnp.float32).astype(jnp.bfloat16)
    update = jnp.dot(mixed, right_root, preferred_element_type=jnp.float32).astype(jnp.bfloat16)
    return (left_new, right_new, update)
```

```python
import math

import jax
import jax.numpy as jnp
from jax import lax
from jax.sharding import PartitionSpec as P

HQ = 4096
DIN = 8192


stat_decay = 0.9


def slot_index(row_counts, tile_rows, capacity):
    offsets = jnp.cumsum(row_counts) - row_counts
    target = jnp.arange(tile_rows, dtype=jnp.int32)
    covered = target[:, None] >= offsets[None, :]
    source = jnp.sum(covered.astype(jnp.int32), axis=1) - 1
    begins = jnp.max(jnp.where(covered, offsets[None, :], 0), axis=1)
    return source * capacity + target - begins


def shards(flat_gradient, range_rows, left_stat, right_stat, left_root, right_root):
    row_count = lax.axis_size("row")
    col_count = lax.axis_size("col")
    row_index = lax.axis_index("row")
    tile_rows = HQ // row_count
    tile_cols = DIN // col_count
    slice_rows = tile_rows // col_count
    block_cols = DIN // row_count
    capacity = flat_gradient.shape[2] // DIN
    held_rows = flat_gradient.reshape(capacity, DIN)
    received = lax.all_to_all(held_rows, "col", split_axis=1, concat_axis=0, tiled=True)
    row_counts = lax.dynamic_index_in_dim(range_rows, row_index, 0, keepdims=False)
    grad_tile = jnp.take(received, slot_index(row_counts, tile_rows, capacity), axis=0)
    row_slice = lax.all_to_all(grad_tile, "col", split_axis=0, concat_axis=1, tiled=True)
    block_piece = lax.all_to_all(row_slice, "row", split_axis=1, concat_axis=0, tiled=True)
    row_block = lax.all_gather(block_piece, "col", axis=0, tiled=True)
    column_panel = lax.all_gather(grad_tile, "row", axis=0, tiled=True)
    left_part = lax.dot_general(
        grad_tile, column_panel, (((1,), (1,)), ((), ())), preferred_element_type=jnp.float32
    )
    left_sum = lax.psum_scatter(
        left_part.astype(jnp.bfloat16), "col", scatter_dimension=1, tiled=True
    ).astype(jnp.float32)
    panel_reordered = (
        column_panel.reshape(row_count, col_count, slice_rows, tile_cols)
        .transpose(1, 0, 2, 3)
        .reshape(HQ, tile_cols)
    )
    right_gram = lax.dot_general(
        panel_reordered, row_block, (((0,), (0,)), ((), ())), preferred_element_type=jnp.float32
    )
    right_new = stat_decay * right_stat + right_gram * (1.0 / math.sqrt(HQ))
    left_mixed = jnp.dot(left_root, column_panel, preferred_element_type=jnp.float32).astype(
        jnp.bfloat16
    )
    update_sum = lax.dot_general(
        lax.all_gather(left_mixed, "col", axis=1, tiled=True),
        right_root,
        (((1,), (1,)), ((), ())),
        preferred_element_type=jnp.float32,
    )
    left_new = stat_decay * left_stat + left_sum * (1.0 / math.sqrt(DIN))
    return (left_new, right_new, update_sum.astype(jnp.bfloat16))


def solution(mesh):
    in_specs = (
        P("row", "col", None),
        P(),
        P("row", "col"),
        P("col", "row"),
        P("row", None),
        P("col", None),
    )
    out_specs = (P("row", "col"), P("col", "row"), P("row", "col"))
    return jax.shard_map(shards, mesh=mesh, in_specs=in_specs, out_specs=out_specs, check_vma=False)
```

```python
import math

import jax
import jax.numpy as jnp
from jax import lax
from jax.sharding import Mesh
from jax.sharding import PartitionSpec as P

HQ = 4096
DIN = 8192


stat_decay = 0.9

COL = ("chip", "core")


def slot_index(row_counts, tile_rows, capacity):
    offsets = jnp.cumsum(row_counts) - row_counts
    target = jnp.arange(tile_rows, dtype=jnp.int32)
    covered = target[:, None] >= offsets[None, :]
    source = jnp.sum(covered.astype(jnp.int32), axis=1) - 1
    begins = jnp.max(jnp.where(covered, offsets[None, :], 0), axis=1)
    return source * capacity + target - begins


def partner(block):
    return lax.ppermute(block, "core", [(0, 1), (1, 0)])


def gather_col(block):
    own = lax.all_gather(block, "chip", axis=0, tiled=False)
    other = partner(own)
    core = lax.axis_index("core")
    both = jnp.stack([own, other])
    return jnp.where(core == 0, both, both[::-1])


def shards(flat_gradient, range_rows, left_stat, right_stat, left_root, right_root):
    row_count = lax.axis_size("row")
    chip_count = lax.axis_size("chip")
    col_count = chip_count * 2
    row_index = lax.axis_index("row")
    core = lax.axis_index("core")
    tile_rows = HQ // row_count
    tile_cols = DIN // col_count
    slice_rows = tile_rows // col_count
    block_cols = DIN // row_count
    chunk = HQ // col_count
    capacity = flat_gradient.shape[2] // DIN
    held_rows = flat_gradient.reshape(capacity, DIN)
    received = lax.all_to_all(held_rows, COL, split_axis=1, concat_axis=0, tiled=True)
    row_counts = lax.dynamic_index_in_dim(range_rows, row_index, 0, keepdims=False)
    grad_tile = jnp.take(received, slot_index(row_counts, tile_rows, capacity), axis=0)
    row_slice = lax.all_to_all(grad_tile, COL, split_axis=0, concat_axis=1, tiled=True)
    block_piece = lax.all_to_all(row_slice, "row", split_axis=1, concat_axis=0, tiled=True)
    row_block = gather_col(block_piece).reshape(HQ, block_cols)
    column_panel = lax.all_gather(grad_tile, "row", axis=0, tiled=True)
    left_part = lax.dot_general(
        grad_tile, column_panel, (((1,), (1,)), ((), ())), preferred_element_type=jnp.float32
    ).reshape(tile_rows, chip_count, 2, chunk)
    keep = lax.dynamic_index_in_dim(left_part, core, 2, keepdims=False)
    send = lax.dynamic_index_in_dim(left_part, 1 - core, 2, keepdims=False)
    chip_sum = keep + partner(send)
    left_sum = lax.psum_scatter(
        chip_sum.astype(jnp.bfloat16), "chip", scatter_dimension=1, tiled=True
    ).reshape(tile_rows, chunk).astype(jnp.float32)
    panel_reordered = (
        column_panel.reshape(row_count, chip_count, 2, slice_rows, tile_cols)
        .transpose(2, 1, 0, 3, 4)
        .reshape(HQ, tile_cols)
    )
    right_gram = lax.dot_general(
        panel_reordered, row_block, (((0,), (0,)), ((), ())), preferred_element_type=jnp.float32
    )
    right_new = stat_decay * right_stat + right_gram * (1.0 / math.sqrt(HQ))
    left_mixed = jnp.dot(left_root, column_panel, preferred_element_type=jnp.float32).astype(
        jnp.bfloat16
    )
    mixed_parts = gather_col(left_mixed)
    mixed_rows = mixed_parts.transpose(2, 1, 0, 3).reshape(tile_rows, DIN)
    update_sum = lax.dot_general(
        mixed_rows,
        right_root,
        (((1,), (1,)), ((), ())),
        preferred_element_type=jnp.float32,
    )
    left_new = stat_decay * left_stat + left_sum * (1.0 / math.sqrt(DIN))
    return (left_new, right_new, update_sum.astype(jnp.bfloat16))


def solution(mesh):
    rows, cols = mesh.devices.shape
    split_mesh = Mesh(mesh.devices.reshape(rows, cols // 2, 2), ("row", "chip", "core"))
    in_specs = (
        P("row", COL, None),
        P(),
        P("row", COL),
        P(COL, "row"),
        P("row", None),
        P(COL, None),
    )
    out_specs = (P("row", COL), P(COL, "row"), P("row", COL))
    return jax.shard_map(
        shards, mesh=split_mesh, in_specs=in_specs, out_specs=out_specs, check_vma=False
    )
```

```python
import math

import jax
import jax.numpy as jnp
from jax import lax
from jax.sharding import Mesh
from jax.sharding import PartitionSpec as P

HQ = 4096
DIN = 8192


stat_decay = 0.9

COL = ("chip", "core")


def slot_index(row_counts, tile_rows, capacity):
    offsets = jnp.cumsum(row_counts) - row_counts
    target = jnp.arange(tile_rows, dtype=jnp.int32)
    covered = target[:, None] >= offsets[None, :]
    source = jnp.sum(covered.astype(jnp.int32), axis=1) - 1
    begins = jnp.max(jnp.where(covered, offsets[None, :], 0), axis=1)
    return source * capacity + target - begins


def partner(block):
    return lax.ppermute(block, "core", [(0, 1), (1, 0)])


def shards(flat_gradient, range_rows, left_stat, right_stat, left_root, right_root):
    row_count = lax.axis_size("row")
    chip_count = lax.axis_size("chip")
    col_count = chip_count * 2
    row_index = lax.axis_index("row")
    core = lax.axis_index("core")
    tile_rows = HQ // row_count
    tile_cols = DIN // col_count
    slice_rows = tile_rows // col_count
    block_cols = DIN // row_count
    chunk = HQ // col_count
    capacity = flat_gradient.shape[2] // DIN
    held_rows = flat_gradient.reshape(capacity, DIN)
    received = lax.all_to_all(held_rows, COL, split_axis=1, concat_axis=0, tiled=True)
    row_counts = lax.dynamic_index_in_dim(range_rows, row_index, 0, keepdims=False)
    grad_tile = jnp.take(received, slot_index(row_counts, tile_rows, capacity), axis=0)
    row_slice = lax.all_to_all(grad_tile, COL, split_axis=0, concat_axis=1, tiled=True)
    block_piece = lax.all_to_all(row_slice, "row", split_axis=1, concat_axis=0, tiled=True)
    row_block = lax.all_gather(block_piece, COL, axis=0, tiled=True)
    shifted_tiles = [grad_tile] + [
        lax.ppermute(grad_tile, "row", [(i, (i + s) % row_count) for i in range(row_count)])
        for s in range(1, row_count)
    ]
    order = (row_index - jnp.arange(row_count, dtype=jnp.int32)) % row_count
    column_panel = jnp.take(jnp.stack(shifted_tiles), order, axis=0).reshape(HQ, tile_cols)
    panel_chunks = column_panel.reshape(chip_count, 2, chunk, tile_cols)
    keep_rows = lax.dynamic_index_in_dim(panel_chunks, core, 1, keepdims=False)
    send_rows = lax.dynamic_index_in_dim(panel_chunks, 1 - core, 1, keepdims=False)
    contract = (((1,), (2,)), ((), ()))
    keep = lax.dot_general(grad_tile, keep_rows, contract, preferred_element_type=jnp.float32)
    send = lax.dot_general(grad_tile, send_rows, contract, preferred_element_type=jnp.float32)
    chip_sum = keep + partner(send.astype(jnp.bfloat16)).astype(jnp.float32)
    left_sum = lax.psum_scatter(
        chip_sum.astype(jnp.bfloat16), "chip", scatter_dimension=1, tiled=True
    ).reshape(tile_rows, chunk).astype(jnp.float32)
    panel_reordered = (
        column_panel.reshape(row_count, col_count, slice_rows, tile_cols)
        .transpose(1, 0, 2, 3)
        .reshape(HQ, tile_cols)
    )
    right_gram = lax.dot_general(
        panel_reordered, row_block, (((0,), (0,)), ((), ())), preferred_element_type=jnp.float32
    )
    right_new = stat_decay * right_stat + right_gram * (1.0 / math.sqrt(HQ))
    left_mixed = jnp.dot(left_root, column_panel, preferred_element_type=jnp.float32).astype(
        jnp.bfloat16
    )
    update_sum = lax.dot_general(
        lax.all_gather(left_mixed, COL, axis=1, tiled=True),
        right_root,
        (((1,), (1,)), ((), ())),
        preferred_element_type=jnp.float32,
    )
    left_new = stat_decay * left_stat + left_sum * (1.0 / math.sqrt(DIN))
    return (left_new, right_new, update_sum.astype(jnp.bfloat16))


def solution(mesh):
    rows, cols = mesh.devices.shape
    split_mesh = Mesh(mesh.devices.reshape(rows, cols // 2, 2), ("row", "chip", "core"))
    in_specs = (
        P("row", COL, None),
        P(),
        P("row", COL),
        P(COL, "row"),
        P("row", None),
        P(COL, None),
    )
    out_specs = (P("row", COL), P(COL, "row"), P("row", COL))
    return jax.shard_map(
        shards, mesh=split_mesh, in_specs=in_specs, out_specs=out_specs, check_vma=False
    )
```

```python
import math

import jax
import jax.numpy as jnp
from jax import lax
from jax.sharding import Mesh
from jax.sharding import PartitionSpec as P

HQ = 4096
DIN = 8192


stat_decay = 0.9

COL = ("chip", "core")


def slot_index(row_counts, tile_rows, capacity):
    offsets = jnp.cumsum(row_counts) - row_counts
    target = jnp.arange(tile_rows, dtype=jnp.int32)
    covered = target[:, None] >= offsets[None, :]
    source = jnp.sum(covered.astype(jnp.int32), axis=1) - 1
    begins = jnp.max(jnp.where(covered, offsets[None, :], 0), axis=1)
    return source * capacity + target - begins


def partner(block):
    return lax.ppermute(block, "core", [(0, 1), (1, 0)])


def shards(flat_gradient, range_rows, left_stat, right_stat, left_root, right_root):
    row_count = lax.axis_size("row")
    chip_count = lax.axis_size("chip")
    col_count = chip_count * 2
    row_index = lax.axis_index("row")
    core = lax.axis_index("core")
    tile_rows = HQ // row_count
    tile_cols = DIN // col_count
    slice_rows = tile_rows // col_count
    block_cols = DIN // row_count
    chunk = HQ // col_count
    capacity = flat_gradient.shape[2] // DIN
    held_rows = flat_gradient.reshape(capacity, DIN)
    received = lax.all_to_all(held_rows, COL, split_axis=1, concat_axis=0, tiled=True)
    row_counts = lax.dynamic_index_in_dim(range_rows, row_index, 0, keepdims=False)
    grad_tile = jnp.take(received, slot_index(row_counts, tile_rows, capacity), axis=0)
    row_slice = lax.all_to_all(grad_tile, COL, split_axis=0, concat_axis=1, tiled=True)
    block_piece = lax.all_to_all(row_slice, "row", split_axis=1, concat_axis=0, tiled=True)
    shifted_tiles = [grad_tile] + [
        lax.ppermute(grad_tile, "row", [(i, (i + s) % row_count) for i in range(row_count)])
        for s in range(1, row_count)
    ]
    order = (row_index - jnp.arange(row_count, dtype=jnp.int32)) % row_count
    column_panel = jnp.take(jnp.stack(shifted_tiles), order, axis=0).reshape(HQ, tile_cols)
    panel_chunks = column_panel.reshape(chip_count, 2, chunk, tile_cols)
    keep_rows = lax.dynamic_index_in_dim(panel_chunks, core, 1, keepdims=False)
    send_rows = lax.dynamic_index_in_dim(panel_chunks, 1 - core, 1, keepdims=False)
    contract = (((1,), (2,)), ((), ()))
    keep = lax.dot_general(grad_tile, keep_rows, contract, preferred_element_type=jnp.float32)
    send = lax.dot_general(grad_tile, send_rows, contract, preferred_element_type=jnp.float32)
    chip_sum = keep + partner(send.astype(jnp.bfloat16)).astype(jnp.float32)
    left_sum = lax.psum_scatter(
        chip_sum.astype(jnp.bfloat16), "chip", scatter_dimension=1, tiled=True
    ).reshape(tile_rows, chunk).astype(jnp.float32)
    panel_reordered = (
        column_panel.reshape(row_count, col_count, slice_rows, tile_cols)
        .transpose(1, 0, 2, 3)
        .reshape(HQ, tile_cols)
    )
    left_mixed = jnp.dot(left_root, column_panel, preferred_element_type=jnp.float32).astype(
        jnp.bfloat16
    )
    gathered = lax.all_gather(
        jnp.stack([block_piece, left_mixed.reshape(block_piece.shape)]), COL, axis=0, tiled=False
    )
    row_block = gathered[:, 0].reshape(HQ, block_cols)
    mixed_rows = (
        gathered[:, 1].reshape(col_count, tile_rows, tile_cols).transpose(1, 0, 2).reshape(tile_rows, DIN)
    )
    right_gram = lax.dot_general(
        panel_reordered, row_block, (((0,), (0,)), ((), ())), preferred_element_type=jnp.float32
    )
    right_new = stat_decay * right_stat + right_gram * (1.0 / math.sqrt(HQ))
    update_sum = lax.dot_general(
        mixed_rows,
        right_root,
        (((1,), (1,)), ((), ())),
        preferred_element_type=jnp.float32,
    )
    left_new = stat_decay * left_stat + left_sum * (1.0 / math.sqrt(DIN))
    return (left_new, right_new, update_sum.astype(jnp.bfloat16))


def solution(mesh):
    rows, cols = mesh.devices.shape
    split_mesh = Mesh(mesh.devices.reshape(rows, cols // 2, 2), ("row", "chip", "core"))
    in_specs = (
        P("row", COL, None),
        P(),
        P("row", COL),
        P(COL, "row"),
        P("row", None),
        P(COL, None),
    )
    out_specs = (P("row", COL), P(COL, "row"), P("row", COL))
    return jax.shard_map(
        shards, mesh=split_mesh, in_specs=in_specs, out_specs=out_specs, check_vma=False
    )
```

```python
import math

import jax
import jax.numpy as jnp
from jax import lax
from jax.sharding import Mesh
from jax.sharding import PartitionSpec as P

HQ = 4096
DIN = 8192


stat_decay = 0.9

COL = ("chip", "core")


def slot_index(row_counts, tile_rows, capacity):
    offsets = jnp.cumsum(row_counts) - row_counts
    target = jnp.arange(tile_rows, dtype=jnp.int32)
    covered = target[:, None] >= offsets[None, :]
    source = jnp.sum(covered.astype(jnp.int32), axis=1) - 1
    begins = jnp.max(jnp.where(covered, offsets[None, :], 0), axis=1)
    return source * capacity + target - begins


def partner(block):
    return lax.ppermute(block, "core", [(0, 1), (1, 0)])


def shards(flat_gradient, range_rows, left_stat, right_stat, left_root, right_root):
    row_count = lax.axis_size("row")
    chip_count = lax.axis_size("chip")
    col_count = chip_count * 2
    row_index = lax.axis_index("row")
    core = lax.axis_index("core")
    tile_rows = HQ // row_count
    tile_cols = DIN // col_count
    slice_rows = tile_rows // col_count
    block_cols = DIN // row_count
    chunk = HQ // col_count
    capacity = flat_gradient.shape[2] // DIN
    held_rows = flat_gradient.reshape(capacity, DIN)
    received = lax.all_to_all(held_rows, COL, split_axis=1, concat_axis=0, tiled=True)
    row_counts = lax.dynamic_index_in_dim(range_rows, row_index, 0, keepdims=False)
    grad_tile = jnp.take(received, slot_index(row_counts, tile_rows, capacity), axis=0)
    col_index = lax.axis_index(COL)
    device_count = row_count * col_count
    pieces = []
    for k in range(col_count):
        target_col = (col_index + k + 2 * row_index) % col_count
        piece = lax.dynamic_slice_in_dim(grad_tile, target_col * slice_rows, slice_rows, 0)
        route = []
        for source in range(device_count):
            r, c = divmod(source, col_count)
            route.append((source, (c // 2) * col_count + (c + k + 2 * r) % col_count))
        pieces.append(lax.ppermute(piece, ("row", "chip", "core"), route))
    source_rows = jnp.arange(row_count, dtype=jnp.int32)[:, None]
    halves = jnp.arange(2, dtype=jnp.int32)[None, :]
    arrival = (col_index - 2 * row_index - halves - 2 * source_rows) % col_count
    block_piece = (
        jnp.take(jnp.stack(pieces), arrival, axis=0)
        .transpose(0, 2, 1, 3)
        .reshape(row_count * slice_rows, block_cols)
    )
    row_block = lax.all_gather(block_piece, COL, axis=0, tiled=True)
    column_panel = lax.all_to_all(
        jnp.broadcast_to(grad_tile[None], (row_count,) + grad_tile.shape),
        "row",
        split_axis=0,
        concat_axis=0,
        tiled=True,
    ).reshape(HQ, tile_cols)
    panel_chunks = column_panel.reshape(chip_count, 2, chunk, tile_cols)
    keep_rows = lax.dynamic_index_in_dim(panel_chunks, core, 1, keepdims=False)
    send_rows = lax.dynamic_index_in_dim(panel_chunks, 1 - core, 1, keepdims=False)
    contract = (((1,), (2,)), ((), ()))
    keep = lax.dot_general(grad_tile, keep_rows, contract, preferred_element_type=jnp.float32)
    send = lax.dot_general(grad_tile, send_rows, contract, preferred_element_type=jnp.float32)
    chip_sum = keep + partner(send.astype(jnp.bfloat16)).astype(jnp.float32)
    left_sum = lax.psum_scatter(
        chip_sum.astype(jnp.bfloat16), "chip", scatter_dimension=1, tiled=True
    ).reshape(tile_rows, chunk).astype(jnp.float32)
    panel_reordered = (
        column_panel.reshape(row_count, col_count, slice_rows, tile_cols)
        .transpose(1, 0, 2, 3)
        .reshape(HQ, tile_cols)
    )
    right_gram = lax.dot_general(
        panel_reordered, row_block, (((0,), (0,)), ((), ())), preferred_element_type=jnp.float32
    )
    right_new = stat_decay * right_stat + right_gram * (1.0 / math.sqrt(HQ))
    left_mixed = jnp.dot(left_root, column_panel, preferred_element_type=jnp.float32).astype(
        jnp.bfloat16
    )
    update_sum = lax.dot_general(
        lax.all_gather(left_mixed, COL, axis=1, tiled=True),
        right_root,
        (((1,), (1,)), ((), ())),
        preferred_element_type=jnp.float32,
    )
    left_new = stat_decay * left_stat + left_sum * (1.0 / math.sqrt(DIN))
    return (left_new, right_new, update_sum.astype(jnp.bfloat16))


def solution(mesh):
    rows, cols = mesh.devices.shape
    split_mesh = Mesh(mesh.devices.reshape(rows, cols // 2, 2), ("row", "chip", "core"))
    in_specs = (
        P("row", COL, None),
        P(),
        P("row", COL),
        P(COL, "row"),
        P("row", None),
        P(COL, None),
    )
    out_specs = (P("row", COL), P(COL, "row"), P("row", COL))
    return jax.shard_map(
        shards, mesh=split_mesh, in_specs=in_specs, out_specs=out_specs, check_vma=False
    )
```

```python
import math

import jax
import jax.numpy as jnp
from jax import lax
from jax.sharding import Mesh
from jax.sharding import PartitionSpec as P

HQ = 4096
DIN = 8192


stat_decay = 0.9

COL = ("chip", "core")
ROW = ("x", "yh")


def slot_index(row_counts, tile_rows, capacity):
    offsets = jnp.cumsum(row_counts) - row_counts
    target = jnp.arange(tile_rows, dtype=jnp.int32)
    covered = target[:, None] >= offsets[None, :]
    source = jnp.sum(covered.astype(jnp.int32), axis=1) - 1
    begins = jnp.max(jnp.where(covered, offsets[None, :], 0), axis=1)
    return source * capacity + target - begins


def partner(block):
    return lax.ppermute(block, "core", [(0, 1), (1, 0)])


def shards(flat_gradient, range_rows, left_stat, right_stat, left_root, right_root):
    x_count = lax.axis_size("x")
    row_count = x_count * 2
    chip_count = lax.axis_size("chip")
    col_count = chip_count * 2
    row_index = lax.axis_index(ROW)
    x_index = lax.axis_index("x")
    y_half = lax.axis_index("yh")
    core = lax.axis_index("core")
    tile_rows = HQ // row_count
    tile_cols = DIN // col_count
    slice_rows = tile_rows // col_count
    block_cols = DIN // row_count
    chunk = HQ // col_count
    capacity = flat_gradient.shape[2] // DIN
    held_rows = flat_gradient.reshape(capacity, DIN)
    received = lax.all_to_all(held_rows, COL, split_axis=1, concat_axis=0, tiled=True)
    row_counts = lax.dynamic_index_in_dim(range_rows, row_index, 0, keepdims=False)
    grad_tile = jnp.take(received, slot_index(row_counts, tile_rows, capacity), axis=0)
    row_slice = lax.all_to_all(grad_tile, COL, split_axis=0, concat_axis=1, tiled=True)
    block_piece = lax.all_to_all(row_slice, ROW, split_axis=1, concat_axis=0, tiled=True)
    row_block = lax.all_gather(block_piece, COL, axis=0, tiled=True)
    other_half = lax.ppermute(grad_tile, "yh", [(0, 1), (1, 0)])
    first = jnp.where(y_half == 0, grad_tile, other_half)
    second = jnp.where(y_half == 0, other_half, grad_tile)
    pair = jnp.stack([first, second])
    panel_parts = jnp.zeros((row_count, tile_rows, tile_cols), grad_tile.dtype)
    panel_parts = lax.dynamic_update_slice_in_dim(panel_parts, pair, 2 * x_index, 0)
    for s in range(1, x_count):
        moved = lax.ppermute(pair, "x", [(i, (i + s) % x_count) for i in range(x_count)])
        panel_parts = lax.dynamic_update_slice_in_dim(
            panel_parts, moved, 2 * ((x_index - s) % x_count), 0
        )
    column_panel = panel_parts.reshape(HQ, tile_cols)
    panel_chunks = column_panel.reshape(chip_count, 2, chunk, tile_cols)
    keep_rows = lax.dynamic_index_in_dim(panel_chunks, core, 1, keepdims=False)
    send_rows = lax.dynamic_index_in_dim(panel_chunks, 1 - core, 1, keepdims=False)
    contract = (((1,), (2,)), ((), ()))
    keep = lax.dot_general(grad_tile, keep_rows, contract, preferred_element_type=jnp.float32)
    send = lax.dot_general(grad_tile, send_rows, contract, preferred_element_type=jnp.float32)
    chip_sum = keep + partner(send.astype(jnp.bfloat16)).astype(jnp.float32)
    left_sum = lax.psum_scatter(
        chip_sum.astype(jnp.bfloat16), "chip", scatter_dimension=1, tiled=True
    ).reshape(tile_rows, chunk).astype(jnp.float32)
    panel_reordered = (
        column_panel.reshape(row_count, col_count, slice_rows, tile_cols)
        .transpose(1, 0, 2, 3)
        .reshape(HQ, tile_cols)
    )
    right_gram = lax.dot_general(
        panel_reordered, row_block, (((0,), (0,)), ((), ())), preferred_element_type=jnp.float32
    )
    right_new = stat_decay * right_stat + right_gram * (1.0 / math.sqrt(HQ))
    left_mixed = jnp.dot(left_root, column_panel, preferred_element_type=jnp.float32).astype(
        jnp.bfloat16
    )
    update_sum = lax.dot_general(
        lax.all_gather(left_mixed, COL, axis=1, tiled=True),
        right_root,
        (((1,), (1,)), ((), ())),
        preferred_element_type=jnp.float32,
    )
    left_new = stat_decay * left_stat + left_sum * (1.0 / math.sqrt(DIN))
    return (left_new, right_new, update_sum.astype(jnp.bfloat16))


def solution(mesh):
    rows, cols = mesh.devices.shape
    split_mesh = Mesh(
        mesh.devices.reshape(rows // 2, 2, cols // 2, 2), ("x", "yh", "chip", "core")
    )
    in_specs = (
        P(ROW, COL, None),
        P(),
        P(ROW, COL),
        P(COL, ROW),
        P(ROW, None),
        P(COL, None),
    )
    out_specs = (P(ROW, COL), P(COL, ROW), P(ROW, COL))
    return jax.shard_map(
        shards, mesh=split_mesh, in_specs=in_specs, out_specs=out_specs, check_vma=False
    )
```

```python
import math

import jax
import jax.numpy as jnp
from jax import lax
from jax.sharding import Mesh
from jax.sharding import PartitionSpec as P

HQ = 4096
DIN = 8192


stat_decay = 0.9

COL = ("chip", "core")
ROW = ("x", "yh")


def slot_index(row_counts, tile_rows, capacity):
    offsets = jnp.cumsum(row_counts) - row_counts
    target = jnp.arange(tile_rows, dtype=jnp.int32)
    covered = target[:, None] >= offsets[None, :]
    source = jnp.sum(covered.astype(jnp.int32), axis=1) - 1
    begins = jnp.max(jnp.where(covered, offsets[None, :], 0), axis=1)
    return source * capacity + target - begins


def partner(block):
    return lax.ppermute(block, "core", [(0, 1), (1, 0)])


def shards(flat_gradient, range_rows, left_stat, right_stat, left_root, right_root):
    x_count = lax.axis_size("x")
    row_count = x_count * 2
    chip_count = lax.axis_size("chip")
    col_count = chip_count * 2
    row_index = lax.axis_index(ROW)
    x_index = lax.axis_index("x")
    y_half = lax.axis_index("yh")
    core = lax.axis_index("core")
    tile_rows = HQ // row_count
    tile_cols = DIN // col_count
    slice_rows = tile_rows // col_count
    block_cols = DIN // row_count
    chunk = HQ // col_count
    capacity = flat_gradient.shape[2] // DIN
    held_rows = flat_gradient.reshape(capacity, DIN)
    received = lax.all_to_all(held_rows, COL, split_axis=1, concat_axis=0, tiled=True)
    row_counts = lax.dynamic_index_in_dim(range_rows, row_index, 0, keepdims=False)
    grad_tile = jnp.take(received, slot_index(row_counts, tile_rows, capacity), axis=0)
    row_slice = lax.all_to_all(grad_tile, COL, split_axis=0, concat_axis=1, tiled=True)
    block_piece = lax.all_to_all(row_slice, ROW, split_axis=1, concat_axis=0, tiled=True)
    row_block = lax.all_to_all(
        jnp.broadcast_to(block_piece[None], (col_count,) + block_piece.shape),
        COL,
        split_axis=0,
        concat_axis=0,
        tiled=True,
    ).reshape(HQ, block_cols)
    other_half = lax.ppermute(grad_tile, "yh", [(0, 1), (1, 0)])
    first = jnp.where(y_half == 0, grad_tile, other_half)
    second = jnp.where(y_half == 0, other_half, grad_tile)
    pair = jnp.stack([first, second])
    panel_parts = jnp.zeros((row_count, tile_rows, tile_cols), grad_tile.dtype)
    panel_parts = lax.dynamic_update_slice_in_dim(panel_parts, pair, 2 * x_index, 0)
    for s in range(1, x_count):
        moved = lax.ppermute(pair, "x", [(i, (i + s) % x_count) for i in range(x_count)])
        panel_parts = lax.dynamic_update_slice_in_dim(
            panel_parts, moved, 2 * ((x_index - s) % x_count), 0
        )
    column_panel = panel_parts.reshape(HQ, tile_cols)
    panel_chunks = column_panel.reshape(chip_count, 2, chunk, tile_cols)
    keep_rows = lax.dynamic_index_in_dim(panel_chunks, core, 1, keepdims=False)
    send_rows = lax.dynamic_index_in_dim(panel_chunks, 1 - core, 1, keepdims=False)
    contract = (((1,), (2,)), ((), ()))
    keep = lax.dot_general(grad_tile, keep_rows, contract, preferred_element_type=jnp.float32)
    send = lax.dot_general(grad_tile, send_rows, contract, preferred_element_type=jnp.float32)
    chip_sum = keep + partner(send.astype(jnp.bfloat16)).astype(jnp.float32)
    left_sum = lax.psum_scatter(
        chip_sum.astype(jnp.bfloat16), "chip", scatter_dimension=1, tiled=True
    ).reshape(tile_rows, chunk).astype(jnp.float32)
    panel_reordered = (
        column_panel.reshape(row_count, col_count, slice_rows, tile_cols)
        .transpose(1, 0, 2, 3)
        .reshape(HQ, tile_cols)
    )
    right_gram = lax.dot_general(
        panel_reordered, row_block, (((0,), (0,)), ((), ())), preferred_element_type=jnp.float32
    )
    right_new = stat_decay * right_stat + right_gram * (1.0 / math.sqrt(HQ))
    left_mixed = jnp.dot(left_root, column_panel, preferred_element_type=jnp.float32).astype(
        jnp.bfloat16
    )
    update_sum = lax.dot_general(
        lax.all_gather(left_mixed, COL, axis=1, tiled=True),
        right_root,
        (((1,), (1,)), ((), ())),
        preferred_element_type=jnp.float32,
    )
    left_new = stat_decay * left_stat + left_sum * (1.0 / math.sqrt(DIN))
    return (left_new, right_new, update_sum.astype(jnp.bfloat16))


def solution(mesh):
    rows, cols = mesh.devices.shape
    split_mesh = Mesh(
        mesh.devices.reshape(rows // 2, 2, cols // 2, 2), ("x", "yh", "chip", "core")
    )
    in_specs = (
        P(ROW, COL, None),
        P(),
        P(ROW, COL),
        P(COL, ROW),
        P(ROW, None),
        P(COL, None),
    )
    out_specs = (P(ROW, COL), P(COL, ROW), P(ROW, COL))
    return jax.shard_map(
        shards, mesh=split_mesh, in_specs=in_specs, out_specs=out_specs, check_vma=False
    )
```

```python
import math

import jax
import jax.numpy as jnp
from jax import lax
from jax.sharding import Mesh
from jax.sharding import PartitionSpec as P

HQ = 4096
DIN = 8192


stat_decay = 0.9

COL = ("chip", "core")
ROW = ("x", "yh")


def slot_index(row_counts, tile_rows, capacity):
    offsets = jnp.cumsum(row_counts) - row_counts
    target = jnp.arange(tile_rows, dtype=jnp.int32)
    covered = target[:, None] >= offsets[None, :]
    source = jnp.sum(covered.astype(jnp.int32), axis=1) - 1
    begins = jnp.max(jnp.where(covered, offsets[None, :], 0), axis=1)
    return source * capacity + target - begins


def partner(block):
    return lax.ppermute(block, "core", [(0, 1), (1, 0)])


def shards(flat_gradient, range_rows, left_stat, right_stat, left_root, right_root):
    x_count = lax.axis_size("x")
    row_count = x_count * 2
    chip_count = lax.axis_size("chip")
    col_count = chip_count * 2
    row_index = lax.axis_index(ROW)
    x_index = lax.axis_index("x")
    y_half = lax.axis_index("yh")
    core = lax.axis_index("core")
    tile_rows = HQ // row_count
    tile_cols = DIN // col_count
    slice_rows = tile_rows // col_count
    block_cols = DIN // row_count
    chunk = HQ // col_count
    capacity = flat_gradient.shape[2] // DIN
    held_rows = flat_gradient.reshape(capacity, DIN)
    received = lax.all_to_all(held_rows, COL, split_axis=1, concat_axis=0, tiled=True)
    row_counts = lax.dynamic_index_in_dim(range_rows, row_index, 0, keepdims=False)
    grad_tile = jnp.take(received, slot_index(row_counts, tile_rows, capacity), axis=0)
    row_slice = lax.all_to_all(grad_tile, COL, split_axis=0, concat_axis=1, tiled=True)
    block_piece = lax.all_to_all(row_slice, ROW, split_axis=1, concat_axis=0, tiled=True)
    other_half = lax.ppermute(grad_tile, "yh", [(0, 1), (1, 0)])
    first = jnp.where(y_half == 0, grad_tile, other_half)
    second = jnp.where(y_half == 0, other_half, grad_tile)
    pair = jnp.stack([first, second])
    moved = [
        lax.ppermute(pair, "x", [(i, (i + s) % x_count) for i in range(x_count)])
        for s in range(1, x_count)
    ]
    moved, block_piece = lax.optimization_barrier((moved, block_piece))
    panel_parts = jnp.zeros((row_count, tile_rows, tile_cols), grad_tile.dtype)
    panel_parts = lax.dynamic_update_slice_in_dim(panel_parts, pair, 2 * x_index, 0)
    for s in range(1, x_count):
        panel_parts = lax.dynamic_update_slice_in_dim(
            panel_parts, moved[s - 1], 2 * ((x_index - s) % x_count), 0
        )
    row_block = lax.all_gather(block_piece, COL, axis=0, tiled=True)
    column_panel = panel_parts.reshape(HQ, tile_cols)
    panel_chunks = column_panel.reshape(chip_count, 2, chunk, tile_cols)
    keep_rows = lax.dynamic_index_in_dim(panel_chunks, core, 1, keepdims=False)
    send_rows = lax.dynamic_index_in_dim(panel_chunks, 1 - core, 1, keepdims=False)
    contract = (((1,), (2,)), ((), ()))
    keep = lax.dot_general(grad_tile, keep_rows, contract, preferred_element_type=jnp.float32)
    send = lax.dot_general(grad_tile, send_rows, contract, preferred_element_type=jnp.float32)
    chip_sum = keep + partner(send.astype(jnp.bfloat16)).astype(jnp.float32)
    left_sum = lax.psum_scatter(
        chip_sum.astype(jnp.bfloat16), "chip", scatter_dimension=1, tiled=True
    ).reshape(tile_rows, chunk).astype(jnp.float32)
    panel_reordered = (
        column_panel.reshape(row_count, col_count, slice_rows, tile_cols)
        .transpose(1, 0, 2, 3)
        .reshape(HQ, tile_cols)
    )
    right_gram = lax.dot_general(
        panel_reordered, row_block, (((0,), (0,)), ((), ())), preferred_element_type=jnp.float32
    )
    right_new = stat_decay * right_stat + right_gram * (1.0 / math.sqrt(HQ))
    left_mixed = jnp.dot(left_root, column_panel, preferred_element_type=jnp.float32).astype(
        jnp.bfloat16
    )
    update_sum = lax.dot_general(
        lax.all_gather(left_mixed, COL, axis=1, tiled=True),
        right_root,
        (((1,), (1,)), ((), ())),
        preferred_element_type=jnp.float32,
    )
    left_new = stat_decay * left_stat + left_sum * (1.0 / math.sqrt(DIN))
    return (left_new, right_new, update_sum.astype(jnp.bfloat16))


def solution(mesh):
    rows, cols = mesh.devices.shape
    split_mesh = Mesh(
        mesh.devices.reshape(rows // 2, 2, cols // 2, 2), ("x", "yh", "chip", "core")
    )
    in_specs = (
        P(ROW, COL, None),
        P(),
        P(ROW, COL),
        P(COL, ROW),
        P(ROW, None),
        P(COL, None),
    )
    out_specs = (P(ROW, COL), P(COL, ROW), P(ROW, COL))
    return jax.shard_map(
        shards, mesh=split_mesh, in_specs=in_specs, out_specs=out_specs, check_vma=False
    )
```

```python
import math

import jax
import jax.numpy as jnp
from jax import lax
from jax.sharding import Mesh
from jax.sharding import PartitionSpec as P

HQ = 4096
DIN = 8192


stat_decay = 0.9

COL = ("chip", "core")
ROW = ("x", "yh")


def slot_index(row_counts, tile_rows, capacity):
    offsets = jnp.cumsum(row_counts) - row_counts
    target = jnp.arange(tile_rows, dtype=jnp.int32)
    covered = target[:, None] >= offsets[None, :]
    source = jnp.sum(covered.astype(jnp.int32), axis=1) - 1
    begins = jnp.max(jnp.where(covered, offsets[None, :], 0), axis=1)
    return source * capacity + target - begins


def partner(block):
    return lax.ppermute(block, "core", [(0, 1), (1, 0)])


def shards(flat_gradient, range_rows, left_stat, right_stat, left_root, right_root):
    x_count = lax.axis_size("x")
    row_count = x_count * 2
    chip_count = lax.axis_size("chip")
    col_count = chip_count * 2
    row_index = lax.axis_index(ROW)
    x_index = lax.axis_index("x")
    y_half = lax.axis_index("yh")
    core = lax.axis_index("core")
    tile_rows = HQ // row_count
    tile_cols = DIN // col_count
    slice_rows = tile_rows // col_count
    block_cols = DIN // row_count
    chunk = HQ // col_count
    capacity = flat_gradient.shape[2] // DIN
    held_rows = flat_gradient.reshape(capacity, DIN)
    received = lax.all_to_all(held_rows, COL, split_axis=1, concat_axis=0, tiled=True)
    row_counts = lax.dynamic_index_in_dim(range_rows, row_index, 0, keepdims=False)
    grad_tile = jnp.take(received, slot_index(row_counts, tile_rows, capacity), axis=0)
    row_slice = lax.all_to_all(grad_tile, COL, split_axis=0, concat_axis=1, tiled=True)
    block_piece = lax.all_to_all(row_slice, ROW, split_axis=1, concat_axis=0, tiled=True)
    other_half = lax.ppermute(grad_tile, "yh", [(0, 1), (1, 0)])
    first = jnp.where(y_half == 0, grad_tile, other_half)
    second = jnp.where(y_half == 0, other_half, grad_tile)
    pair = jnp.stack([first, second])
    moved = [
        lax.ppermute(pair, "x", [(i, (i + s) % x_count) for i in range(x_count)])
        for s in range(1, x_count)
    ]
    row_block = lax.all_gather(block_piece, COL, axis=0, tiled=True)
    moved, row_block = lax.optimization_barrier((moved, row_block))
    panel_parts = jnp.zeros((row_count, tile_rows, tile_cols), grad_tile.dtype)
    panel_parts = lax.dynamic_update_slice_in_dim(panel_parts, pair, 2 * x_index, 0)
    for s in range(1, x_count):
        panel_parts = lax.dynamic_update_slice_in_dim(
            panel_parts, moved[s - 1], 2 * ((x_index - s) % x_count), 0
        )
    column_panel = panel_parts.reshape(HQ, tile_cols)
    panel_chunks = column_panel.reshape(chip_count, 2, chunk, tile_cols)
    keep_rows = lax.dynamic_index_in_dim(panel_chunks, core, 1, keepdims=False)
    send_rows = lax.dynamic_index_in_dim(panel_chunks, 1 - core, 1, keepdims=False)
    contract = (((1,), (2,)), ((), ()))
    keep = lax.dot_general(grad_tile, keep_rows, contract, preferred_element_type=jnp.float32)
    send = lax.dot_general(grad_tile, send_rows, contract, preferred_element_type=jnp.float32)
    chip_sum = keep + partner(send.astype(jnp.bfloat16)).astype(jnp.float32)
    left_sum = lax.psum_scatter(
        chip_sum.astype(jnp.bfloat16), "chip", scatter_dimension=1, tiled=True
    ).reshape(tile_rows, chunk).astype(jnp.float32)
    panel_reordered = (
        column_panel.reshape(row_count, col_count, slice_rows, tile_cols)
        .transpose(1, 0, 2, 3)
        .reshape(HQ, tile_cols)
    )
    right_gram = lax.dot_general(
        panel_reordered, row_block, (((0,), (0,)), ((), ())), preferred_element_type=jnp.float32
    )
    right_new = stat_decay * right_stat + right_gram * (1.0 / math.sqrt(HQ))
    left_mixed = jnp.dot(left_root, column_panel, preferred_element_type=jnp.float32).astype(
        jnp.bfloat16
    )
    update_sum = lax.dot_general(
        lax.all_gather(left_mixed, COL, axis=1, tiled=True),
        right_root,
        (((1,), (1,)), ((), ())),
        preferred_element_type=jnp.float32,
    )
    left_new = stat_decay * left_stat + left_sum * (1.0 / math.sqrt(DIN))
    return (left_new, right_new, update_sum.astype(jnp.bfloat16))


def solution(mesh):
    rows, cols = mesh.devices.shape
    split_mesh = Mesh(
        mesh.devices.reshape(rows // 2, 2, cols // 2, 2), ("x", "yh", "chip", "core")
    )
    in_specs = (
        P(ROW, COL, None),
        P(),
        P(ROW, COL),
        P(COL, ROW),
        P(ROW, None),
        P(COL, None),
    )
    out_specs = (P(ROW, COL), P(COL, ROW), P(ROW, COL))
    return jax.shard_map(
        shards, mesh=split_mesh, in_specs=in_specs, out_specs=out_specs, check_vma=False
    )
```

```python
import math

import jax
import jax.numpy as jnp
from jax import lax
from jax.sharding import Mesh
from jax.sharding import PartitionSpec as P

HQ = 4096
DIN = 8192


stat_decay = 0.9

COL = ("chip", "core")
ROW = ("x", "yh")


def slot_index(row_counts, tile_rows, capacity):
    offsets = jnp.cumsum(row_counts) - row_counts
    target = jnp.arange(tile_rows, dtype=jnp.int32)
    covered = target[:, None] >= offsets[None, :]
    source = jnp.sum(covered.astype(jnp.int32), axis=1) - 1
    begins = jnp.max(jnp.where(covered, offsets[None, :], 0), axis=1)
    return source * capacity + target - begins


def partner(block):
    return lax.ppermute(block, "core", [(0, 1), (1, 0)])


def shards(flat_gradient, range_rows, left_stat, right_stat, left_root, right_root):
    x_count = lax.axis_size("x")
    row_count = x_count * 2
    chip_count = lax.axis_size("chip")
    col_count = chip_count * 2
    row_index = lax.axis_index(ROW)
    x_index = lax.axis_index("x")
    y_half = lax.axis_index("yh")
    core = lax.axis_index("core")
    tile_rows = HQ // row_count
    tile_cols = DIN // col_count
    slice_rows = tile_rows // col_count
    block_cols = DIN // row_count
    chunk = HQ // col_count
    capacity = flat_gradient.shape[2] // DIN
    held_rows = flat_gradient.reshape(capacity, DIN)
    received = lax.all_to_all(held_rows, COL, split_axis=1, concat_axis=0, tiled=True)
    row_counts = lax.dynamic_index_in_dim(range_rows, row_index, 0, keepdims=False)
    grad_tile = jnp.take(received, slot_index(row_counts, tile_rows, capacity), axis=0)
    row_slice = lax.all_to_all(grad_tile, COL, split_axis=0, concat_axis=1, tiled=True)
    block_piece = lax.all_to_all(row_slice, ROW, split_axis=1, concat_axis=0, tiled=True)
    other_half = lax.ppermute(grad_tile, "yh", [(0, 1), (1, 0)])
    first = jnp.where(y_half == 0, grad_tile, other_half)
    second = jnp.where(y_half == 0, other_half, grad_tile)
    pair = jnp.stack([first, second])
    moved = [
        lax.ppermute(pair, "x", [(i, (i + s) % x_count) for i in range(x_count)])
        for s in range(1, x_count)
    ]
    row_block = lax.all_gather(block_piece, COL, axis=0, tiled=True)
    moved, row_block = lax.optimization_barrier((moved, row_block))
    panel_parts = jnp.zeros((row_count, tile_rows, tile_cols), grad_tile.dtype)
    panel_parts = lax.dynamic_update_slice_in_dim(panel_parts, pair, 2 * x_index, 0)
    for s in range(1, x_count):
        panel_parts = lax.dynamic_update_slice_in_dim(
            panel_parts, moved[s - 1], 2 * ((x_index - s) % x_count), 0
        )
    column_panel = panel_parts.reshape(HQ, tile_cols)
    col_index = lax.axis_index(COL)
    sub = jnp.arange(chunk, dtype=jnp.int32)
    sub_index = (
        ((col_index % 2) * (col_count // 2) + sub // slice_rows) * (row_count * slice_rows)
        + (col_index // 2) * slice_rows
        + sub % slice_rows
    )
    sub_rows = jnp.take(row_block, sub_index, axis=0)
    left_part = lax.dot_general(
        row_block, sub_rows, (((1,), (1,)), ((), ())), preferred_element_type=jnp.float32
    ).astype(jnp.bfloat16)
    left_part = (
        left_part.reshape(col_count, row_count, slice_rows, chunk).transpose(1, 0, 2, 3).reshape(HQ, chunk)
    )
    left_sum = lax.psum_scatter(left_part, ROW, scatter_dimension=0, tiled=True).astype(jnp.float32)
    panel_reordered = (
        column_panel.reshape(row_count, col_count, slice_rows, tile_cols)
        .transpose(1, 0, 2, 3)
        .reshape(HQ, tile_cols)
    )
    right_gram = lax.dot_general(
        panel_reordered, row_block, (((0,), (0,)), ((), ())), preferred_element_type=jnp.float32
    )
    right_new = stat_decay * right_stat + right_gram * (1.0 / math.sqrt(HQ))
    left_mixed = jnp.dot(left_root, column_panel, preferred_element_type=jnp.float32).astype(
        jnp.bfloat16
    )
    update_sum = lax.dot_general(
        lax.all_gather(left_mixed, COL, axis=1, tiled=True),
        right_root,
        (((1,), (1,)), ((), ())),
        preferred_element_type=jnp.float32,
    )
    left_new = stat_decay * left_stat + left_sum * (1.0 / math.sqrt(DIN))
    return (left_new, right_new, update_sum.astype(jnp.bfloat16))


def solution(mesh):
    rows, cols = mesh.devices.shape
    split_mesh = Mesh(
        mesh.devices.reshape(rows // 2, 2, cols // 2, 2), ("x", "yh", "chip", "core")
    )
    in_specs = (
        P(ROW, COL, None),
        P(),
        P(ROW, COL),
        P(COL, ROW),
        P(ROW, None),
        P(COL, None),
    )
    out_specs = (P(ROW, COL), P(COL, ROW), P(ROW, COL))
    return jax.shard_map(
        shards, mesh=split_mesh, in_specs=in_specs, out_specs=out_specs, check_vma=False
    )
```

```python
import math

import jax
import jax.numpy as jnp
from jax import lax
from jax.sharding import Mesh
from jax.sharding import PartitionSpec as P

HQ = 4096
DIN = 8192


stat_decay = 0.9

COL = ("chip", "core")
ROW = ("x", "yh")


def slot_index(row_counts, tile_rows, capacity):
    offsets = jnp.cumsum(row_counts) - row_counts
    target = jnp.arange(tile_rows, dtype=jnp.int32)
    covered = target[:, None] >= offsets[None, :]
    source = jnp.sum(covered.astype(jnp.int32), axis=1) - 1
    begins = jnp.max(jnp.where(covered, offsets[None, :], 0), axis=1)
    return source * capacity + target - begins


def partner(block):
    return lax.ppermute(block, "core", [(0, 1), (1, 0)])


def shards(flat_gradient, range_rows, left_stat, right_stat, left_root, right_root):
    x_count = lax.axis_size("x")
    row_count = x_count * 2
    chip_count = lax.axis_size("chip")
    col_count = chip_count * 2
    row_index = lax.axis_index(ROW)
    x_index = lax.axis_index("x")
    y_half = lax.axis_index("yh")
    core = lax.axis_index("core")
    tile_rows = HQ // row_count
    tile_cols = DIN // col_count
    slice_rows = tile_rows // col_count
    block_cols = DIN // row_count
    chunk = HQ // col_count
    capacity = flat_gradient.shape[2] // DIN
    held_rows = flat_gradient.reshape(capacity, DIN)
    received = lax.all_to_all(held_rows, COL, split_axis=1, concat_axis=0, tiled=True)
    row_counts = lax.dynamic_index_in_dim(range_rows, row_index, 0, keepdims=False)
    grad_tile = jnp.take(received, slot_index(row_counts, tile_rows, capacity), axis=0)
    row_slice = lax.all_to_all(grad_tile, COL, split_axis=0, concat_axis=1, tiled=True)
    block_piece = lax.all_to_all(row_slice, ROW, split_axis=1, concat_axis=0, tiled=True)
    other_half = lax.ppermute(grad_tile, "yh", [(0, 1), (1, 0)])
    first = jnp.where(y_half == 0, grad_tile, other_half)
    second = jnp.where(y_half == 0, other_half, grad_tile)
    pair = jnp.stack([first, second])
    moved = [
        lax.ppermute(pair, "x", [(i, (i + s) % x_count) for i in range(x_count)])
        for s in range(1, x_count)
    ]
    row_block = lax.all_gather(block_piece, COL, axis=0, tiled=True)
    moved, row_block = lax.optimization_barrier((moved, row_block))
    panel_parts = jnp.zeros((row_count, tile_rows, tile_cols), grad_tile.dtype)
    panel_parts = lax.dynamic_update_slice_in_dim(panel_parts, pair, 2 * x_index, 0)
    for s in range(1, x_count):
        panel_parts = lax.dynamic_update_slice_in_dim(
            panel_parts, moved[s - 1], 2 * ((x_index - s) % x_count), 0
        )
    column_panel = panel_parts.reshape(HQ, tile_cols)
    panel_chunks = column_panel.reshape(chip_count, 2, chunk, tile_cols)
    keep_rows = lax.dynamic_index_in_dim(panel_chunks, core, 1, keepdims=False)
    send_rows = lax.dynamic_index_in_dim(panel_chunks, 1 - core, 1, keepdims=False)
    contract = (((1,), (2,)), ((), ()))
    keep = lax.dot_general(grad_tile, keep_rows, contract, preferred_element_type=jnp.float32)
    send = lax.dot_general(grad_tile, send_rows, contract, preferred_element_type=jnp.float32)
    chip_sum = keep + partner(send.astype(jnp.bfloat16)).astype(jnp.float32)
    chip_index = lax.axis_index("chip")
    outgoing = chip_sum.astype(jnp.bfloat16).transpose(1, 0, 2)
    incoming = [
        lax.ppermute(
            lax.dynamic_index_in_dim(outgoing, (chip_index + s) % chip_count, 0, keepdims=False),
            "chip",
            [(i, (i + s) % chip_count) for i in range(chip_count)],
        )
        for s in range(1, chip_count)
    ]
    panel_reordered = (
        column_panel.reshape(row_count, col_count, slice_rows, tile_cols)
        .transpose(1, 0, 2, 3)
        .reshape(HQ, tile_cols)
    )
    right_gram = lax.dot_general(
        panel_reordered, row_block, (((0,), (0,)), ((), ())), preferred_element_type=jnp.float32
    )
    right_new = stat_decay * right_stat + right_gram * (1.0 / math.sqrt(HQ))
    left_mixed = jnp.dot(left_root, column_panel, preferred_element_type=jnp.float32).astype(
        jnp.bfloat16
    )
    mixed_rows = lax.all_gather(left_mixed, COL, axis=1, tiled=True)
    incoming, mixed_rows = lax.optimization_barrier((incoming, mixed_rows))
    left_sum = lax.dynamic_index_in_dim(chip_sum, chip_index, 1, keepdims=False)
    for part in incoming:
        left_sum = left_sum + part.astype(jnp.float32)
    update_sum = lax.dot_general(
        mixed_rows,
        right_root,
        (((1,), (1,)), ((), ())),
        preferred_element_type=jnp.float32,
    )
    left_new = stat_decay * left_stat + left_sum * (1.0 / math.sqrt(DIN))
    return (left_new, right_new, update_sum.astype(jnp.bfloat16))


def solution(mesh):
    rows, cols = mesh.devices.shape
    split_mesh = Mesh(
        mesh.devices.reshape(rows // 2, 2, cols // 2, 2), ("x", "yh", "chip", "core")
    )
    in_specs = (
        P(ROW, COL, None),
        P(),
        P(ROW, COL),
        P(COL, ROW),
        P(ROW, None),
        P(COL, None),
    )
    out_specs = (P(ROW, COL), P(COL, ROW), P(ROW, COL))
    return jax.shard_map(
        shards, mesh=split_mesh, in_specs=in_specs, out_specs=out_specs, check_vma=False
    )
```

```python
import math

import jax
import jax.numpy as jnp
from jax import lax
from jax.sharding import Mesh
from jax.sharding import PartitionSpec as P

HQ = 4096
DIN = 8192


stat_decay = 0.9

COL = ("chip", "core")
ROW = ("x", "yh")


def slot_index(row_counts, tile_rows, capacity):
    offsets = jnp.cumsum(row_counts) - row_counts
    target = jnp.arange(tile_rows, dtype=jnp.int32)
    covered = target[:, None] >= offsets[None, :]
    source = jnp.sum(covered.astype(jnp.int32), axis=1) - 1
    begins = jnp.max(jnp.where(covered, offsets[None, :], 0), axis=1)
    return source * capacity + target - begins


def partner(block):
    return lax.ppermute(block, "core", [(0, 1), (1, 0)])


def shards(flat_gradient, range_rows, left_stat, right_stat, left_root, right_root):
    x_count = lax.axis_size("x")
    row_count = x_count * 2
    chip_count = lax.axis_size("chip")
    col_count = chip_count * 2
    row_index = lax.axis_index(ROW)
    x_index = lax.axis_index("x")
    y_half = lax.axis_index("yh")
    core = lax.axis_index("core")
    tile_rows = HQ // row_count
    tile_cols = DIN // col_count
    slice_rows = tile_rows // col_count
    block_cols = DIN // row_count
    chunk = HQ // col_count
    capacity = flat_gradient.shape[2] // DIN
    held_rows = flat_gradient.reshape(capacity, DIN)
    received = lax.all_to_all(held_rows, COL, split_axis=1, concat_axis=0, tiled=True)
    row_counts = lax.dynamic_index_in_dim(range_rows, row_index, 0, keepdims=False)
    grad_tile = jnp.take(received, slot_index(row_counts, tile_rows, capacity), axis=0)
    row_slice = lax.all_to_all(grad_tile, COL, split_axis=0, concat_axis=1, tiled=True)
    block_piece = lax.all_to_all(row_slice, ROW, split_axis=1, concat_axis=0, tiled=True)
    other_half = lax.ppermute(grad_tile, "yh", [(0, 1), (1, 0)])
    first = jnp.where(y_half == 0, grad_tile, other_half)
    second = jnp.where(y_half == 0, other_half, grad_tile)
    pair = jnp.stack([first, second])
    moved = [
        lax.ppermute(pair, "x", [(i, (i + s) % x_count) for i in range(x_count)])
        for s in range(1, x_count)
    ]
    row_block = lax.all_gather(block_piece, COL, axis=0, tiled=True)
    moved, row_block = lax.optimization_barrier((moved, row_block))
    panel_parts = jnp.zeros((row_count, tile_rows, tile_cols), grad_tile.dtype)
    panel_parts = lax.dynamic_update_slice_in_dim(panel_parts, pair, 2 * x_index, 0)
    for s in range(1, x_count):
        panel_parts = lax.dynamic_update_slice_in_dim(
            panel_parts, moved[s - 1], 2 * ((x_index - s) % x_count), 0
        )
    column_panel = panel_parts.reshape(HQ, tile_cols)
    panel_chunks = column_panel.reshape(chip_count, 2, chunk, tile_cols)
    keep_rows = lax.dynamic_index_in_dim(panel_chunks, core, 1, keepdims=False)
    send_rows = lax.dynamic_index_in_dim(panel_chunks, 1 - core, 1, keepdims=False)
    contract = (((1,), (2,)), ((), ()))
    keep = lax.dot_general(grad_tile, keep_rows, contract, preferred_element_type=jnp.float32)
    send = lax.dot_general(grad_tile, send_rows, contract, preferred_element_type=jnp.float32)
    chip_sum = keep + partner(send.astype(jnp.bfloat16)).astype(jnp.float32)
    chip_index = lax.axis_index("chip")
    outgoing = chip_sum.astype(jnp.bfloat16).transpose(1, 0, 2)
    incoming = [
        lax.ppermute(
            lax.dynamic_index_in_dim(outgoing, (chip_index + s) % chip_count, 0, keepdims=False),
            "chip",
            [(i, (i + s) % chip_count) for i in range(chip_count)],
        )
        for s in range(1, chip_count)
    ]
    panel_reordered = (
        column_panel.reshape(row_count, col_count, slice_rows, tile_cols)
        .transpose(1, 0, 2, 3)
        .reshape(HQ, tile_cols)
    )
    right_gram = lax.dot_general(
        panel_reordered, row_block, (((0,), (0,)), ((), ())), preferred_element_type=jnp.float32
    )
    right_new = stat_decay * right_stat + right_gram * (1.0 / math.sqrt(HQ))
    left_mixed = jnp.dot(left_root, column_panel, preferred_element_type=jnp.float32).astype(
        jnp.bfloat16
    )
    own_mixed = lax.all_gather(left_mixed, "chip", axis=1, tiled=True)
    incoming, own_mixed = lax.optimization_barrier((incoming, own_mixed))
    other_mixed = partner(own_mixed)
    left_sum = lax.dynamic_index_in_dim(chip_sum, chip_index, 1, keepdims=False)
    for part in incoming:
        left_sum = left_sum + part.astype(jnp.float32)
    root_blocks = right_root.reshape(tile_cols, chip_count, 2, tile_cols)
    own_root = lax.dynamic_index_in_dim(root_blocks, core, 2, keepdims=False).reshape(tile_cols, DIN // 2)
    other_root = lax.dynamic_index_in_dim(root_blocks, 1 - core, 2, keepdims=False).reshape(
        tile_cols, DIN // 2
    )
    contract_cols = (((1,), (1,)), ((), ()))
    update_sum = lax.dot_general(
        own_mixed, own_root, contract_cols, preferred_element_type=jnp.float32
    ) + lax.dot_general(other_mixed, other_root, contract_cols, preferred_element_type=jnp.float32)
    left_new = stat_decay * left_stat + left_sum * (1.0 / math.sqrt(DIN))
    return (left_new, right_new, update_sum.astype(jnp.bfloat16))


def solution(mesh):
    rows, cols = mesh.devices.shape
    split_mesh = Mesh(
        mesh.devices.reshape(rows // 2, 2, cols // 2, 2), ("x", "yh", "chip", "core")
    )
    in_specs = (
        P(ROW, COL, None),
        P(),
        P(ROW, COL),
        P(COL, ROW),
        P(ROW, None),
        P(COL, None),
    )
    out_specs = (P(ROW, COL), P(COL, ROW), P(ROW, COL))
    return jax.shard_map(
        shards, mesh=split_mesh, in_specs=in_specs, out_specs=out_specs, check_vma=False
    )
```

```python
import math

import jax
import jax.numpy as jnp
from jax import lax
from jax.sharding import Mesh
from jax.sharding import PartitionSpec as P

HQ = 4096
DIN = 8192


stat_decay = 0.9

COL = ("chip", "core")
ROW = ("x", "yh")


def slot_index(row_counts, tile_rows, capacity):
    offsets = jnp.cumsum(row_counts) - row_counts
    target = jnp.arange(tile_rows, dtype=jnp.int32)
    covered = target[:, None] >= offsets[None, :]
    source = jnp.sum(covered.astype(jnp.int32), axis=1) - 1
    begins = jnp.max(jnp.where(covered, offsets[None, :], 0), axis=1)
    return source * capacity + target - begins


def partner(block):
    return lax.ppermute(block, "core", [(0, 1), (1, 0)])


def shards(flat_gradient, range_rows, left_stat, right_stat, left_root, right_root):
    x_count = lax.axis_size("x")
    row_count = x_count * 2
    chip_count = lax.axis_size("chip")
    col_count = chip_count * 2
    row_index = lax.axis_index(ROW)
    x_index = lax.axis_index("x")
    y_half = lax.axis_index("yh")
    core = lax.axis_index("core")
    tile_rows = HQ // row_count
    tile_cols = DIN // col_count
    slice_rows = tile_rows // col_count
    block_cols = DIN // row_count
    chunk = HQ // col_count
    capacity = flat_gradient.shape[2] // DIN
    held_rows = flat_gradient.reshape(capacity, DIN)
    received = lax.all_to_all(held_rows, COL, split_axis=1, concat_axis=0, tiled=True)
    row_counts = lax.dynamic_index_in_dim(range_rows, row_index, 0, keepdims=False)
    grad_tile = jnp.take(received, slot_index(row_counts, tile_rows, capacity), axis=0)
    row_slice = lax.all_to_all(grad_tile, COL, split_axis=0, concat_axis=1, tiled=True)
    block_piece = lax.all_to_all(row_slice, ROW, split_axis=1, concat_axis=0, tiled=True)
    other_half = lax.ppermute(grad_tile, "yh", [(0, 1), (1, 0)])
    first = jnp.where(y_half == 0, grad_tile, other_half)
    second = jnp.where(y_half == 0, other_half, grad_tile)
    pair = jnp.stack([first, second])
    moved = [
        lax.ppermute(pair, "x", [(i, (i + s) % x_count) for i in range(x_count)])
        for s in range(1, x_count)
    ]
    row_block = lax.all_gather(block_piece, COL, axis=0, tiled=True)
    moved, row_block = lax.optimization_barrier((moved, row_block))
    panel_parts = jnp.zeros((row_count, tile_rows, tile_cols), grad_tile.dtype)
    panel_parts = lax.dynamic_update_slice_in_dim(panel_parts, pair, 2 * x_index, 0)
    for s in range(1, x_count):
        panel_parts = lax.dynamic_update_slice_in_dim(
            panel_parts, moved[s - 1], 2 * ((x_index - s) % x_count), 0
        )
    column_panel = panel_parts.reshape(HQ, tile_cols)
    col_index = lax.axis_index(COL)
    sub = jnp.arange(chunk, dtype=jnp.int32)
    sub_index = (
        ((col_index % 2) * (col_count // 2) + sub // slice_rows) * (row_count * slice_rows)
        + (col_index // 2) * slice_rows
        + sub % slice_rows
    )
    sub_rows = jnp.take(row_block, sub_index, axis=0)
    left_part = lax.dot_general(
        row_block, sub_rows, (((1,), (1,)), ((), ())), preferred_element_type=jnp.float32
    )
    left_part = left_part.reshape(col_count, row_count, slice_rows, chunk).transpose(1, 0, 2, 3)
    left_part = left_part.reshape(row_count, tile_rows, chunk)
    outgoing = left_part.astype(jnp.bfloat16)
    incoming = [
        lax.ppermute(
            lax.dynamic_index_in_dim(outgoing, (row_index + s) % row_count, 0, keepdims=False),
            ROW,
            [(i, (i + s) % row_count) for i in range(row_count)],
        )
        for s in range(1, row_count)
    ]
    panel_reordered = (
        column_panel.reshape(row_count, col_count, slice_rows, tile_cols)
        .transpose(1, 0, 2, 3)
        .reshape(HQ, tile_cols)
    )
    right_gram = lax.dot_general(
        panel_reordered, row_block, (((0,), (0,)), ((), ())), preferred_element_type=jnp.float32
    )
    right_new = stat_decay * right_stat + right_gram * (1.0 / math.sqrt(HQ))
    left_mixed = jnp.dot(left_root, column_panel, preferred_element_type=jnp.float32).astype(
        jnp.bfloat16
    )
    mixed_rows = lax.all_gather(left_mixed, COL, axis=1, tiled=True)
    incoming, mixed_rows = lax.optimization_barrier((incoming, mixed_rows))
    left_sum = lax.dynamic_index_in_dim(left_part, row_index, 0, keepdims=False)
    for part in incoming:
        left_sum = left_sum + part.astype(jnp.float32)
    update_sum = lax.dot_general(
        mixed_rows,
        right_root,
        (((1,), (1,)), ((), ())),
        preferred_element_type=jnp.float32,
    )
    left_new = stat_decay * left_stat + left_sum * (1.0 / math.sqrt(DIN))
    return (left_new, right_new, update_sum.astype(jnp.bfloat16))


def solution(mesh):
    rows, cols = mesh.devices.shape
    split_mesh = Mesh(
        mesh.devices.reshape(rows // 2, 2, cols // 2, 2), ("x", "yh", "chip", "core")
    )
    in_specs = (
        P(ROW, COL, None),
        P(),
        P(ROW, COL),
        P(COL, ROW),
        P(ROW, None),
        P(COL, None),
    )
    out_specs = (P(ROW, COL), P(COL, ROW), P(ROW, COL))
    return jax.shard_map(
        shards, mesh=split_mesh, in_specs=in_specs, out_specs=out_specs, check_vma=False
    )
```

```python
import math

import jax
import jax.numpy as jnp
from jax import lax
from jax.sharding import Mesh
from jax.sharding import PartitionSpec as P

HQ = 4096
DIN = 8192


stat_decay = 0.9

COL = ("chip", "core")
ROW = ("x", "yh")


def slot_index(row_counts, tile_rows, capacity):
    offsets = jnp.cumsum(row_counts) - row_counts
    target = jnp.arange(tile_rows, dtype=jnp.int32)
    covered = target[:, None] >= offsets[None, :]
    source = jnp.sum(covered.astype(jnp.int32), axis=1) - 1
    begins = jnp.max(jnp.where(covered, offsets[None, :], 0), axis=1)
    return source * capacity + target - begins


def partner(block):
    return lax.ppermute(block, "core", [(0, 1), (1, 0)])


def shards(flat_gradient, range_rows, left_stat, right_stat, left_root, right_root):
    x_count = lax.axis_size("x")
    row_count = x_count * 2
    chip_count = lax.axis_size("chip")
    col_count = chip_count * 2
    row_index = lax.axis_index(ROW)
    x_index = lax.axis_index("x")
    y_half = lax.axis_index("yh")
    core = lax.axis_index("core")
    tile_rows = HQ // row_count
    tile_cols = DIN // col_count
    slice_rows = tile_rows // col_count
    block_cols = DIN // row_count
    chunk = HQ // col_count
    capacity = flat_gradient.shape[2] // DIN
    held_rows = flat_gradient.reshape(capacity, DIN)
    received = lax.all_to_all(held_rows, COL, split_axis=1, concat_axis=0, tiled=True)
    row_counts = lax.dynamic_index_in_dim(range_rows, row_index, 0, keepdims=False)
    grad_tile = jnp.take(received, slot_index(row_counts, tile_rows, capacity), axis=0)
    row_slice = lax.all_to_all(grad_tile, COL, split_axis=0, concat_axis=1, tiled=True)
    block_piece = lax.all_to_all(row_slice, ROW, split_axis=1, concat_axis=0, tiled=True)
    other_half = lax.ppermute(grad_tile, "yh", [(0, 1), (1, 0)])
    first = jnp.where(y_half == 0, grad_tile, other_half)
    second = jnp.where(y_half == 0, other_half, grad_tile)
    pair = jnp.stack([first, second])
    moved = [
        lax.ppermute(pair, "x", [(i, (i + s) % x_count) for i in range(x_count)])
        for s in range(1, x_count)
    ]
    row_block = lax.all_gather(block_piece, COL, axis=0, tiled=True)
    moved, row_block = lax.optimization_barrier((moved, row_block))
    panel_parts = jnp.zeros((row_count, tile_rows, tile_cols), grad_tile.dtype)
    panel_parts = lax.dynamic_update_slice_in_dim(panel_parts, pair, 2 * x_index, 0)
    for s in range(1, x_count):
        panel_parts = lax.dynamic_update_slice_in_dim(
            panel_parts, moved[s - 1], 2 * ((x_index - s) % x_count), 0
        )
    column_panel = panel_parts.reshape(HQ, tile_cols)
    col_index = lax.axis_index(COL)
    sub = jnp.arange(chunk, dtype=jnp.int32)
    sub_index = (
        ((col_index % 2) * (col_count // 2) + sub // slice_rows) * (row_count * slice_rows)
        + (col_index // 2) * slice_rows
        + sub % slice_rows
    )
    sub_rows = jnp.take(row_block, sub_index, axis=0)
    left_part = lax.dot_general(
        row_block, sub_rows, (((1,), (1,)), ((), ())), preferred_element_type=jnp.float32
    )
    left_part = left_part.reshape(col_count, row_count, slice_rows, chunk).transpose(1, 0, 2, 3)
    left_part = left_part.reshape(row_count, tile_rows, chunk)
    incoming = lax.all_to_all(left_part.astype(jnp.bfloat16), ROW, 0, 0, tiled=True)
    panel_reordered = (
        column_panel.reshape(row_count, col_count, slice_rows, tile_cols)
        .transpose(1, 0, 2, 3)
        .reshape(HQ, tile_cols)
    )
    right_gram = lax.dot_general(
        panel_reordered, row_block, (((0,), (0,)), ((), ())), preferred_element_type=jnp.float32
    )
    right_new = stat_decay * right_stat + right_gram * (1.0 / math.sqrt(HQ))
    left_mixed = jnp.dot(left_root, column_panel, preferred_element_type=jnp.float32).astype(
        jnp.bfloat16
    )
    mixed_rows = lax.all_gather(left_mixed, COL, axis=1, tiled=True)
    incoming, mixed_rows = lax.optimization_barrier((incoming, mixed_rows))
    own_part = lax.dynamic_index_in_dim(left_part, row_index, 0, keepdims=False)
    others = jnp.arange(row_count, dtype=jnp.int32)[:, None, None] != row_index
    left_sum = own_part + jnp.sum(
        jnp.where(others, incoming.astype(jnp.float32), 0.0), axis=0
    )
    update_sum = lax.dot_general(
        mixed_rows,
        right_root,
        (((1,), (1,)), ((), ())),
        preferred_element_type=jnp.float32,
    )
    left_new = stat_decay * left_stat + left_sum * (1.0 / math.sqrt(DIN))
    return (left_new, right_new, update_sum.astype(jnp.bfloat16))


def solution(mesh):
    rows, cols = mesh.devices.shape
    split_mesh = Mesh(
        mesh.devices.reshape(rows // 2, 2, cols // 2, 2), ("x", "yh", "chip", "core")
    )
    in_specs = (
        P(ROW, COL, None),
        P(),
        P(ROW, COL),
        P(COL, ROW),
        P(ROW, None),
        P(COL, None),
    )
    out_specs = (P(ROW, COL), P(COL, ROW), P(ROW, COL))
    return jax.shard_map(
        shards, mesh=split_mesh, in_specs=in_specs, out_specs=out_specs, check_vma=False
    )
```

```python
import math

import jax
import jax.numpy as jnp
from jax import lax
from jax.sharding import Mesh
from jax.sharding import PartitionSpec as P

HQ = 4096
DIN = 8192


stat_decay = 0.9

COL = ("chip", "core")
ROW = ("x", "yh")


def slot_index(row_counts, tile_rows, capacity):
    offsets = jnp.cumsum(row_counts) - row_counts
    target = jnp.arange(tile_rows, dtype=jnp.int32)
    covered = target[:, None] >= offsets[None, :]
    source = jnp.sum(covered.astype(jnp.int32), axis=1) - 1
    begins = jnp.max(jnp.where(covered, offsets[None, :], 0), axis=1)
    return source * capacity + target - begins


def partner(block):
    return lax.ppermute(block, "core", [(0, 1), (1, 0)])


def shards(flat_gradient, range_rows, left_stat, right_stat, left_root, right_root):
    x_count = lax.axis_size("x")
    row_count = x_count * 2
    chip_count = lax.axis_size("chip")
    col_count = chip_count * 2
    row_index = lax.axis_index(ROW)
    x_index = lax.axis_index("x")
    y_half = lax.axis_index("yh")
    core = lax.axis_index("core")
    tile_rows = HQ // row_count
    tile_cols = DIN // col_count
    slice_rows = tile_rows // col_count
    block_cols = DIN // row_count
    chunk = HQ // col_count
    capacity = flat_gradient.shape[2] // DIN
    held_rows = flat_gradient.reshape(capacity, DIN)
    received = lax.all_to_all(held_rows, COL, split_axis=1, concat_axis=0, tiled=True)
    row_counts = lax.dynamic_index_in_dim(range_rows, row_index, 0, keepdims=False)
    grad_tile = jnp.take(received, slot_index(row_counts, tile_rows, capacity), axis=0)
    row_slice = lax.all_to_all(grad_tile, COL, split_axis=0, concat_axis=1, tiled=True)
    block_piece = lax.all_to_all(row_slice, ROW, split_axis=1, concat_axis=0, tiled=True)
    other_half = lax.ppermute(grad_tile, "yh", [(0, 1), (1, 0)])
    other_half, block_piece = lax.optimization_barrier((other_half, block_piece))
    first = jnp.where(y_half == 0, grad_tile, other_half)
    second = jnp.where(y_half == 0, other_half, grad_tile)
    pair = jnp.stack([first, second])
    moved = [
        lax.ppermute(pair, "x", [(i, (i + s) % x_count) for i in range(x_count)])
        for s in range(1, x_count)
    ]
    row_block = lax.all_gather(block_piece, COL, axis=0, tiled=True)
    moved, row_block = lax.optimization_barrier((moved, row_block))
    panel_parts = jnp.zeros((row_count, tile_rows, tile_cols), grad_tile.dtype)
    panel_parts = lax.dynamic_update_slice_in_dim(panel_parts, pair, 2 * x_index, 0)
    for s in range(1, x_count):
        panel_parts = lax.dynamic_update_slice_in_dim(
            panel_parts, moved[s - 1], 2 * ((x_index - s) % x_count), 0
        )
    column_panel = panel_parts.reshape(HQ, tile_cols)
    col_index = lax.axis_index(COL)
    sub = jnp.arange(chunk, dtype=jnp.int32)
    sub_index = (
        ((col_index % 2) * (col_count // 2) + sub // slice_rows) * (row_count * slice_rows)
        + (col_index // 2) * slice_rows
        + sub % slice_rows
    )
    sub_rows = jnp.take(row_block, sub_index, axis=0)
    left_part = lax.dot_general(
        row_block, sub_rows, (((1,), (1,)), ((), ())), preferred_element_type=jnp.float32
    )
    left_part = left_part.reshape(col_count, row_count, slice_rows, chunk).transpose(1, 0, 2, 3)
    left_part = left_part.reshape(row_count, tile_rows, chunk)
    outgoing = left_part.astype(jnp.bfloat16)
    incoming = [
        lax.ppermute(
            lax.dynamic_index_in_dim(outgoing, (row_index + s) % row_count, 0, keepdims=False),
            ROW,
            [(i, (i + s) % row_count) for i in range(row_count)],
        )
        for s in range(1, row_count)
    ]
    panel_reordered = (
        column_panel.reshape(row_count, col_count, slice_rows, tile_cols)
        .transpose(1, 0, 2, 3)
        .reshape(HQ, tile_cols)
    )
    right_gram = lax.dot_general(
        panel_reordered, row_block, (((0,), (0,)), ((), ())), preferred_element_type=jnp.float32
    )
    right_new = stat_decay * right_stat + right_gram * (1.0 / math.sqrt(HQ))
    left_mixed = jnp.dot(left_root, column_panel, preferred_element_type=jnp.float32).astype(
        jnp.bfloat16
    )
    mixed_rows = lax.all_gather(left_mixed, COL, axis=1, tiled=True)
    incoming, mixed_rows = lax.optimization_barrier((incoming, mixed_rows))
    left_sum = lax.dynamic_index_in_dim(left_part, row_index, 0, keepdims=False)
    for part in incoming:
        left_sum = left_sum + part.astype(jnp.float32)
    update_sum = lax.dot_general(
        mixed_rows,
        right_root,
        (((1,), (1,)), ((), ())),
        preferred_element_type=jnp.float32,
    )
    left_new = stat_decay * left_stat + left_sum * (1.0 / math.sqrt(DIN))
    return (left_new, right_new, update_sum.astype(jnp.bfloat16))


def solution(mesh):
    rows, cols = mesh.devices.shape
    split_mesh = Mesh(
        mesh.devices.reshape(rows // 2, 2, cols // 2, 2), ("x", "yh", "chip", "core")
    )
    in_specs = (
        P(ROW, COL, None),
        P(),
        P(ROW, COL),
        P(COL, ROW),
        P(ROW, None),
        P(COL, None),
    )
    out_specs = (P(ROW, COL), P(COL, ROW), P(ROW, COL))
    return jax.shard_map(
        shards, mesh=split_mesh, in_specs=in_specs, out_specs=out_specs, check_vma=False
    )
```

```python
import math

import jax
import jax.numpy as jnp
from jax import lax
from jax.sharding import Mesh
from jax.sharding import PartitionSpec as P

HQ = 4096
DIN = 8192


stat_decay = 0.9

COL = ("chip", "core")
ROW = ("x", "yh")


def slot_index(row_counts, tile_rows, capacity):
    offsets = jnp.cumsum(row_counts) - row_counts
    target = jnp.arange(tile_rows, dtype=jnp.int32)
    covered = target[:, None] >= offsets[None, :]
    source = jnp.sum(covered.astype(jnp.int32), axis=1) - 1
    begins = jnp.max(jnp.where(covered, offsets[None, :], 0), axis=1)
    return source * capacity + target - begins


def partner(block):
    return lax.ppermute(block, "core", [(0, 1), (1, 0)])


def shards(flat_gradient, range_rows, left_stat, right_stat, left_root, right_root):
    x_count = lax.axis_size("x")
    row_count = x_count * 2
    chip_count = lax.axis_size("chip")
    col_count = chip_count * 2
    row_index = lax.axis_index(ROW)
    x_index = lax.axis_index("x")
    y_half = lax.axis_index("yh")
    core = lax.axis_index("core")
    tile_rows = HQ // row_count
    tile_cols = DIN // col_count
    slice_rows = tile_rows // col_count
    block_cols = DIN // row_count
    chunk = HQ // col_count
    capacity = flat_gradient.shape[2] // DIN
    held_rows = flat_gradient.reshape(capacity, DIN)
    received = lax.all_to_all(held_rows, COL, split_axis=1, concat_axis=0, tiled=True)
    row_counts = lax.dynamic_index_in_dim(range_rows, row_index, 0, keepdims=False)
    grad_tile = jnp.take(received, slot_index(row_counts, tile_rows, capacity), axis=0)
    row_slice = lax.all_to_all(grad_tile, COL, split_axis=0, concat_axis=1, tiled=True)
    block_piece = lax.all_to_all(row_slice, ROW, split_axis=1, concat_axis=0, tiled=True)
    other_half = lax.ppermute(grad_tile, "yh", [(0, 1), (1, 0)])
    other_half, block_piece = lax.optimization_barrier((other_half, block_piece))
    first = jnp.where(y_half == 0, grad_tile, other_half)
    second = jnp.where(y_half == 0, other_half, grad_tile)
    pair = jnp.stack([first, second])
    moved = [
        lax.ppermute(pair, "x", [(i, (i + s) % x_count) for i in range(x_count)])
        for s in range(1, x_count)
    ]
    row_block = lax.all_gather(block_piece, COL, axis=0, tiled=True)
    panel_parts = jnp.zeros((row_count, tile_rows, tile_cols), grad_tile.dtype)
    panel_parts = lax.dynamic_update_slice_in_dim(panel_parts, pair, 2 * x_index, 0)
    for s in range(1, x_count):
        panel_parts = lax.dynamic_update_slice_in_dim(
            panel_parts, moved[s - 1], 2 * ((x_index - s) % x_count), 0
        )
    column_panel = panel_parts.reshape(HQ, tile_cols)
    left_mixed = jnp.dot(left_root, column_panel, preferred_element_type=jnp.float32).astype(
        jnp.bfloat16
    )
    column_panel, left_mixed, row_block = lax.optimization_barrier(
        (column_panel, left_mixed, row_block)
    )
    col_index = lax.axis_index(COL)
    sub = jnp.arange(chunk, dtype=jnp.int32)
    sub_index = (
        ((col_index % 2) * (col_count // 2) + sub // slice_rows) * (row_count * slice_rows)
        + (col_index // 2) * slice_rows
        + sub % slice_rows
    )
    sub_rows = jnp.take(row_block, sub_index, axis=0)
    left_part = lax.dot_general(
        row_block, sub_rows, (((1,), (1,)), ((), ())), preferred_element_type=jnp.float32
    )
    left_part = left_part.reshape(col_count, row_count, slice_rows, chunk).transpose(1, 0, 2, 3)
    left_part = left_part.reshape(row_count, tile_rows, chunk)
    outgoing = left_part.astype(jnp.bfloat16)
    incoming = [
        lax.ppermute(
            lax.dynamic_index_in_dim(outgoing, (row_index + s) % row_count, 0, keepdims=False),
            ROW,
            [(i, (i + s) % row_count) for i in range(row_count)],
        )
        for s in range(1, row_count)
    ]
    panel_reordered = (
        column_panel.reshape(row_count, col_count, slice_rows, tile_cols)
        .transpose(1, 0, 2, 3)
        .reshape(HQ, tile_cols)
    )
    right_gram = lax.dot_general(
        panel_reordered, row_block, (((0,), (0,)), ((), ())), preferred_element_type=jnp.float32
    )
    right_new = stat_decay * right_stat + right_gram * (1.0 / math.sqrt(HQ))
    mixed_rows = lax.all_gather(left_mixed, COL, axis=1, tiled=True)
    incoming, mixed_rows = lax.optimization_barrier((incoming, mixed_rows))
    left_sum = lax.dynamic_index_in_dim(left_part, row_index, 0, keepdims=False)
    for part in incoming:
        left_sum = left_sum + part.astype(jnp.float32)
    update_sum = lax.dot_general(
        mixed_rows,
        right_root,
        (((1,), (1,)), ((), ())),
        preferred_element_type=jnp.float32,
    )
    left_new = stat_decay * left_stat + left_sum * (1.0 / math.sqrt(DIN))
    return (left_new, right_new, update_sum.astype(jnp.bfloat16))


def solution(mesh):
    rows, cols = mesh.devices.shape
    split_mesh = Mesh(
        mesh.devices.reshape(rows // 2, 2, cols // 2, 2), ("x", "yh", "chip", "core")
    )
    in_specs = (
        P(ROW, COL, None),
        P(),
        P(ROW, COL),
        P(COL, ROW),
        P(ROW, None),
        P(COL, None),
    )
    out_specs = (P(ROW, COL), P(COL, ROW), P(ROW, COL))
    return jax.shard_map(
        shards, mesh=split_mesh, in_specs=in_specs, out_specs=out_specs, check_vma=False
    )
```

```python
import math

import jax
import jax.numpy as jnp
from jax import lax
from jax.sharding import Mesh
from jax.sharding import PartitionSpec as P

HQ = 4096
DIN = 8192


stat_decay = 0.9

COL = ("chip", "core")
ROW = ("x", "yh")


def slot_index(row_counts, tile_rows, capacity):
    offsets = jnp.cumsum(row_counts) - row_counts
    target = jnp.arange(tile_rows, dtype=jnp.int32)
    covered = target[:, None] >= offsets[None, :]
    source = jnp.sum(covered.astype(jnp.int32), axis=1) - 1
    begins = jnp.max(jnp.where(covered, offsets[None, :], 0), axis=1)
    return source * capacity + target - begins


def partner(block):
    return lax.ppermute(block, "core", [(0, 1), (1, 0)])


def shards(flat_gradient, range_rows, left_stat, right_stat, left_root, right_root):
    x_count = lax.axis_size("x")
    row_count = x_count * 2
    chip_count = lax.axis_size("chip")
    col_count = chip_count * 2
    row_index = lax.axis_index(ROW)
    x_index = lax.axis_index("x")
    y_half = lax.axis_index("yh")
    core = lax.axis_index("core")
    tile_rows = HQ // row_count
    tile_cols = DIN // col_count
    slice_rows = tile_rows // col_count
    block_cols = DIN // row_count
    chunk = HQ // col_count
    capacity = flat_gradient.shape[2] // DIN
    held_rows = flat_gradient.reshape(capacity, DIN)
    received = lax.all_to_all(held_rows, COL, split_axis=1, concat_axis=0, tiled=True)
    row_counts = lax.dynamic_index_in_dim(range_rows, row_index, 0, keepdims=False)
    grad_tile = jnp.take(received, slot_index(row_counts, tile_rows, capacity), axis=0)
    row_slice = lax.all_to_all(grad_tile, COL, split_axis=0, concat_axis=1, tiled=True)
    block_piece = lax.all_to_all(row_slice, ROW, split_axis=1, concat_axis=0, tiled=True)
    other_half = lax.ppermute(grad_tile, "yh", [(0, 1), (1, 0)])
    other_half, block_piece = lax.optimization_barrier((other_half, block_piece))
    first = jnp.where(y_half == 0, grad_tile, other_half)
    second = jnp.where(y_half == 0, other_half, grad_tile)
    pair = jnp.stack([first, second])
    moved = [
        lax.ppermute(pair, "x", [(i, (i + s) % x_count) for i in range(x_count)])
        for s in range(1, x_count)
    ]
    row_block = lax.all_gather(block_piece, COL, axis=0, tiled=True)
    panel_parts = jnp.zeros((row_count, tile_rows, tile_cols), grad_tile.dtype)
    panel_parts = lax.dynamic_update_slice_in_dim(panel_parts, pair, 2 * x_index, 0)
    for s in range(1, x_count):
        panel_parts = lax.dynamic_update_slice_in_dim(
            panel_parts, moved[s - 1], 2 * ((x_index - s) % x_count), 0
        )
    column_panel = panel_parts.reshape(HQ, tile_cols)
    left_mixed = jnp.dot(left_root, column_panel, preferred_element_type=jnp.float32).astype(
        jnp.bfloat16
    )
    column_panel, left_mixed, row_block = lax.optimization_barrier(
        (column_panel, left_mixed, row_block)
    )
    col_index = lax.axis_index(COL)
    sub = jnp.arange(chunk, dtype=jnp.int32)
    sub_index = (
        ((col_index % 2) * (col_count // 2) + sub // slice_rows) * (row_count * slice_rows)
        + (col_index // 2) * slice_rows
        + sub % slice_rows
    )
    sub_rows = jnp.take(row_block, sub_index, axis=0)
    left_part = lax.dot_general(
        row_block, sub_rows, (((1,), (1,)), ((), ())), preferred_element_type=jnp.float32
    )
    left_part = left_part.reshape(col_count, row_count, slice_rows, chunk).transpose(1, 0, 2, 3)
    left_part = left_part.reshape(row_count, tile_rows, chunk)
    pair_parts = left_part.reshape(x_count, 2, tile_rows, chunk)
    outgoing = pair_parts.astype(jnp.bfloat16)
    incoming = [
        lax.ppermute(
            lax.dynamic_index_in_dim(outgoing, (x_index + s) % x_count, 0, keepdims=False),
            "x",
            [(i, (i + s) % x_count) for i in range(x_count)],
        )
        for s in range(1, x_count)
    ]
    panel_reordered = (
        column_panel.reshape(row_count, col_count, slice_rows, tile_cols)
        .transpose(1, 0, 2, 3)
        .reshape(HQ, tile_cols)
    )
    right_gram = lax.dot_general(
        panel_reordered, row_block, (((0,), (0,)), ((), ())), preferred_element_type=jnp.float32
    )
    right_new = stat_decay * right_stat + right_gram * (1.0 / math.sqrt(HQ))
    mixed_rows = lax.all_gather(left_mixed, COL, axis=1, tiled=True)
    incoming, mixed_rows = lax.optimization_barrier((incoming, mixed_rows))
    x_sum = lax.dynamic_index_in_dim(pair_parts, x_index, 0, keepdims=False)
    for part in incoming:
        x_sum = x_sum + part.astype(jnp.float32)
    across = lax.ppermute(
        lax.dynamic_index_in_dim(x_sum, 1 - y_half, 0, keepdims=False).astype(jnp.bfloat16),
        "yh",
        [(0, 1), (1, 0)],
    )
    left_sum = lax.dynamic_index_in_dim(x_sum, y_half, 0, keepdims=False) + across.astype(jnp.float32)
    update_sum = lax.dot_general(
        mixed_rows,
        right_root,
        (((1,), (1,)), ((), ())),
        preferred_element_type=jnp.float32,
    )
    left_new = stat_decay * left_stat + left_sum * (1.0 / math.sqrt(DIN))
    return (left_new, right_new, update_sum.astype(jnp.bfloat16))


def solution(mesh):
    rows, cols = mesh.devices.shape
    split_mesh = Mesh(
        mesh.devices.reshape(rows // 2, 2, cols // 2, 2), ("x", "yh", "chip", "core")
    )
    in_specs = (
        P(ROW, COL, None),
        P(),
        P(ROW, COL),
        P(COL, ROW),
        P(ROW, None),
        P(COL, None),
    )
    out_specs = (P(ROW, COL), P(COL, ROW), P(ROW, COL))
    return jax.shard_map(
        shards, mesh=split_mesh, in_specs=in_specs, out_specs=out_specs, check_vma=False
    )
```
